256 devices in a mesh: row: 16 (over z_hi, x, core), col: 16 (over z_lo, y).
Axes of the slice: x: 4, y: 4, z: 8 (z_hi: 2, z_lo: 4; z = z_hi * 4 + z_lo), core: 2. Of those that a mesh axis runs over, the one named last changes fastest.
Arguments:
- features: bfloat16 [64, 512, 2048], P(None, 'row', 'col'), may hold values from -6 to 6
- patch_index: int32 [512, 2048], P('row', 'col'), may hold values from 0 to 2047
- confidence: float32 [512, 2048], P('row', 'col'), may hold values from 0.2 to 1
- bank: bfloat16 [256, 576, 2048], P(('row', 'col')), may hold values from -6 to 6
- page_owner: int32 [2], replicated, may hold values from 0 to 255
- texture_weight: bfloat16 [64, 576], replicated, may hold values from -0.25 to 0.25
- conv_weight: bfloat16 [8, 9, 64, 64], replicated, may hold values from -0.25 to 0.25
Outputs:
- restored: bfloat16 [64, 512, 2048], P(None, 'row', 'col')
The draws below stay inside these ranges and needn't reach their ends.
Inputs may be any that keep to these rules, and one draw needn't show every extreme that they name: `patch_index`: each entry is a patch number of the page. `page_owner`: each entry is a slot number.
All inputs are finite; a program needn't handle non-finite values.
Results may differ from the reference program's by a relative error of at most 0.024.
Values may be sent and summed in bfloat16 or wider, within the bound.
No kernel may reach another device: no remote copies, remote signals or barrier semaphores. Data moves between devices by JAX's collectives and lax.ppermute only.
A program may use at most 128 MiB of HBM per device.

```python
import jax
import jax.numpy as jnp
from jax import lax

C = 64
BANKW = 576
PATCHES = 2048
LAYERS = 8
STEPS = 2
SLOTS = 256
HEIGHT = 512
WIDTH = 2048


def set_ends(array, own_key, least, high):
    dims = array.shape
    place = [jax.random.randint(jax.random.fold_in(own_key, axis), (), 0, dims[axis]) for axis in range(len(dims))]
    array = array.at[tuple(place)].set(least)
    longest = dims.index(max(dims))
    place[longest] = (place[longest] + 1) % dims[longest]
    return array.at[tuple(place)].set(high)


def level_of(own_key, shape, pieces, smallest, top_value):
    def one(axis_at, blocks):
        draws = jax.random.uniform(jax.random.fold_in(jax.random.fold_in(own_key, 6), axis_at), (blocks,), jnp.float32, smallest / len(pieces), top_value / len(pieces))
        return jnp.repeat(jnp.exp(draws), shape[axis_at] // blocks).reshape((-1,) + (1,) * (len(shape) - axis_at - 1))

    gain = one(*pieces[0])
    for cut in pieces[1:]:
        gain = gain * one(*cut)
    return gain


def bell_draw(own_key, shape, deviation, reach, split=(), kind=jnp.bfloat16):
    level = level_of(own_key, shape, split, -0.22, 0.18) if split else 1.0
    entries = jax.random.normal(own_key, shape, jnp.float32) * deviation * level
    return jnp.minimum(jnp.maximum(entries, -reach), reach).astype(kind)


def setup_inputs(seed: int = 0) -> dict:
    streams_of = jax.random.split(jax.random.key(seed), 8)
    features = bell_draw(streams_of[0], (C, HEIGHT, WIDTH), 1.0, 6.0, ((1, 16), (2, 16)))
    patch_index = set_ends(jax.random.randint(streams_of[1], (HEIGHT, WIDTH), 0, PATCHES), jax.random.fold_in(streams_of[1], 1), 0, PATCHES - 1).astype(jnp.int32)
    confidence = jnp.clip(0.2 + 0.8 * jax.random.uniform(streams_of[2], (HEIGHT, WIDTH), jnp.float32) ** level_of(streams_of[2], (HEIGHT, WIDTH), ((0, 16), (1, 16)), -0.2, 0.2), 0.2, 1.0)
    bank = bell_draw(streams_of[3], (SLOTS, BANKW, PATCHES), 1.0, 6.0, ((0, 256),))
    page_owner = jax.random.randint(streams_of[4], (STEPS,), 0, SLOTS).astype(jnp.int32)
    texture_weight = bell_draw(streams_of[5], (C, BANKW), BANKW ** -0.5, 0.25)
    conv_weight = bell_draw(streams_of[6], (LAYERS, 9, C, C), (9 * C) ** -0.5, 0.25)
    return {"features": features, "patch_index": patch_index, "confidence": confidence, "bank": bank, "page_owner": page_owner, "texture_weight": texture_weight, "conv_weight": conv_weight}


def convolve(field, kernel):
    taps = kernel.astype(jnp.float32).reshape(3, 3, C, C).transpose(2, 3, 0, 1)
    out = lax.conv_general_dilated(field.astype(jnp.float32)[None], taps, (1, 1), ((1, 1), (1, 1)), dimension_numbers=("NCHW", "OIHW", "NCHW"))
    return out[0]


def reference(features, patch_index, confidence, bank, page_owner, texture_weight, conv_weight):
    state = features
    for step in range(STEPS):
        page = lax.dynamic_index_in_dim(bank, page_owner[step], 0, keepdims=False)
        projected = jnp.dot(texture_weight, page, preferred_element_type=jnp.float32).astype(jnp.bfloat16)
        texture = jnp.take(projected, patch_index.reshape(-1), axis=1).reshape(C, HEIGHT, WIDTH)
        state = (state.astype(jnp.float32) + confidence[None] * texture.astype(jnp.float32)).astype(jnp.bfloat16)
        for block in range(LAYERS // 2):
            inner = jnp.maximum(convolve(state, conv_weight[2 * block]), 0.0).astype(jnp.bfloat16)
            state = (state.astype(jnp.float32) + convolve(inner, conv_weight[2 * block + 1])).astype(jnp.bfloat16)
    return state
```

```python
import jax
import jax.numpy as jnp
from jax import lax
from jax.sharding import PartitionSpec as P

LAYERS = 8
STEPS = 2
HALO = LAYERS


def shift_pairs(n_row, n_col, dr, dc):
    pairs = []
    for r in range(n_row):
        for c in range(n_col):
            tr, tc = r + dr, c + dc
            if 0 <= tr < n_row and 0 <= tc < n_col:
                pairs.append((r * n_col + c, tr * n_col + tc))
    return pairs


def exchange(block, width):
    n_row = lax.axis_size("row")
    n_col = lax.axis_size("col")
    axes = ("row", "col")
    rows = {-1: slice(block.shape[1] - width, None), 0: slice(None), 1: slice(0, width)}
    cols = {-1: slice(block.shape[2] - width, None), 0: slice(None), 1: slice(0, width)}
    got = {}
    for dr in (-1, 0, 1):
        for dc in (-1, 0, 1):
            if dr == 0 and dc == 0:
                continue
            piece = block[:, rows[dr], cols[dc]]
            got[(dr, dc)] = lax.ppermute(piece, axes, shift_pairs(n_row, n_col, -dr, -dc))
    top = jnp.concatenate([got[(-1, -1)], got[(-1, 0)], got[(-1, 1)]], axis=2)
    mid = jnp.concatenate([got[(0, -1)], block, got[(0, 1)]], axis=2)
    bot = jnp.concatenate([got[(1, -1)], got[(1, 0)], got[(1, 1)]], axis=2)
    return jnp.concatenate([top, mid, bot], axis=1)


def broadcast_pages(masked):
    axes = ("row", "col")
    n = lax.axis_size("row") * lax.axis_size("col")
    steps, chans, width = masked.shape
    chunks = masked.reshape(steps, chans, n, width // n).transpose(2, 0, 1, 3)
    mine = lax.all_to_all(chunks, axes, 0, 0, tiled=True)
    total = jnp.sum(mine.astype(jnp.float32), axis=0).astype(masked.dtype)
    spread = jnp.broadcast_to(total[None], (n,) + total.shape)
    back = lax.all_to_all(spread, axes, 0, 0, tiled=True)
    return back.transpose(1, 2, 0, 3).reshape(steps, chans, width)


def conv_valid(field, kernel):
    taps = kernel.reshape(3, 3, kernel.shape[1], kernel.shape[2]).transpose(2, 3, 0, 1)
    out = lax.conv_general_dilated(
        field[None],
        taps,
        (1, 1),
        "VALID",
        dimension_numbers=("NCHW", "OIHW", "NCHW"),
        preferred_element_type=jnp.float32,
    )
    return out[0]


def body(features, patch_index, confidence, bank, page_owner, texture_weight, conv_weight):
    chans, tile_h, tile_w = features.shape
    n_row = lax.axis_size("row")
    n_col = lax.axis_size("col")
    r = lax.axis_index("row")
    c = lax.axis_index("col")
    me = r * n_col + c

    local_proj = jnp.dot(texture_weight, bank[0], preferred_element_type=jnp.float32).astype(jnp.bfloat16)
    masked = jnp.stack(
        [jnp.where(me == page_owner[s], local_proj, jnp.zeros_like(local_proj)) for s in range(STEPS)]
    )
    pages = broadcast_pages(masked)

    ext_rows = r * tile_h - HALO + jnp.arange(tile_h + 2 * HALO)
    ext_cols = c * tile_w - HALO + jnp.arange(tile_w + 2 * HALO)
    row_ok = (ext_rows >= 0) & (ext_rows < n_row * tile_h)
    col_ok = (ext_cols >= 0) & (ext_cols < n_col * tile_w)
    valid = row_ok[:, None] & col_ok[None, :]

    flat_index = patch_index.reshape(-1)
    state = features
    for step in range(STEPS):
        page_rows = pages[step].T
        texture = page_rows[flat_index].T.reshape(chans, tile_h, tile_w)
        state = (state.astype(jnp.float32) + confidence[None] * texture.astype(jnp.float32)).astype(jnp.bfloat16)
        x = exchange(state, HALO)
        halo = HALO
        for block in range(LAYERS // 2):
            inner = jnp.maximum(conv_valid(x, conv_weight[2 * block]), 0.0)
            halo -= 1
            keep = valid[HALO - halo : HALO + tile_h + halo, HALO - halo : HALO + tile_w + halo]
            inner = jnp.where(keep[None], inner, 0.0).astype(jnp.bfloat16)
            res = x[:, 2:-2, 2:-2].astype(jnp.float32) + conv_valid(inner, conv_weight[2 * block + 1])
            halo -= 1
            keep = valid[HALO - halo : HALO + tile_h + halo, HALO - halo : HALO + tile_w + halo]
            x = jnp.where(keep[None], res, 0.0).astype(jnp.bfloat16)
        state = x
    return state


def solution(mesh):
    return jax.shard_map(
        body,
        mesh=mesh,
        in_specs=(
            P(None, "row", "col"),
            P("row", "col"),
            P("row", "col"),
            P(("row", "col"), None, None),
            P(),
            P(),
            P(),
        ),
        out_specs=P(None, "row", "col"),
        check_vma=False,
    )
```

```python
import jax
import jax.numpy as jnp
from jax import lax
from jax.sharding import PartitionSpec as P

LAYERS = 8
STEPS = 2
HALO = LAYERS


def shift_pairs(n_row, n_col, dr, dc):
    pairs = []
    for r in range(n_row):
        for c in range(n_col):
            tr, tc = r + dr, c + dc
            if 0 <= tr < n_row and 0 <= tc < n_col:
                pairs.append((r * n_col + c, tr * n_col + tc))
    return pairs


def exchange(block, width):
    n_row = lax.axis_size("row")
    n_col = lax.axis_size("col")
    axes = ("row", "col")
    rows = {-1: slice(block.shape[1] - width, None), 0: slice(None), 1: slice(0, width)}
    cols = {-1: slice(block.shape[2] - width, None), 0: slice(None), 1: slice(0, width)}
    got = {}
    for dr in (-1, 0, 1):
        for dc in (-1, 0, 1):
            if dr == 0 and dc == 0:
                continue
            piece = block[:, rows[dr], cols[dc]]
            got[(dr, dc)] = lax.ppermute(piece, axes, shift_pairs(n_row, n_col, -dr, -dc))
    top = jnp.concatenate([got[(-1, -1)], got[(-1, 0)], got[(-1, 1)]], axis=2)
    mid = jnp.concatenate([got[(0, -1)], block, got[(0, 1)]], axis=2)
    bot = jnp.concatenate([got[(1, -1)], got[(1, 0)], got[(1, 1)]], axis=2)
    return jnp.concatenate([top, mid, bot], axis=1)


def broadcast_pages(masked):
    axes = ("row", "col")
    n = lax.axis_size("row") * lax.axis_size("col")
    steps, chans, width = masked.shape
    chunks = masked.reshape(steps, chans, n, width // n).transpose(2, 0, 1, 3)
    mine = lax.all_to_all(chunks, axes, 0, 0, tiled=True)
    total = jnp.sum(mine.astype(jnp.float32), axis=0).astype(masked.dtype)
    spread = jnp.broadcast_to(total[None], (n,) + total.shape)
    back = lax.all_to_all(spread, axes, 0, 0, tiled=True)
    return back.transpose(1, 2, 0, 3).reshape(steps, chans, width)


def conv_flat(flat, kernel, pitch):
    chans = flat.shape[0]
    rows = flat.shape[1] // pitch
    n_out = (rows - 2) * pitch
    padded = jnp.pad(flat, ((0, 0), (1, 1)))
    windows = [padded[:, dy * pitch + dx : dy * pitch + dx + n_out] for dy in range(3) for dx in range(3)]
    stacked = jnp.concatenate(windows, axis=0)
    flat_kernel = kernel.transpose(1, 0, 2).reshape(kernel.shape[1], 9 * chans)
    return jnp.dot(flat_kernel, stacked, preferred_element_type=jnp.float32)


def body(features, patch_index, confidence, bank, page_owner, texture_weight, conv_weight):
    chans, tile_h, tile_w = features.shape
    n_row = lax.axis_size("row")
    n_col = lax.axis_size("col")
    r = lax.axis_index("row")
    c = lax.axis_index("col")
    me = r * n_col + c

    local_proj = jnp.dot(texture_weight, bank[0], preferred_element_type=jnp.float32).astype(jnp.bfloat16)
    masked = jnp.stack(
        [jnp.where(me == page_owner[s], local_proj, jnp.zeros_like(local_proj)) for s in range(STEPS)]
    )
    pages = broadcast_pages(masked)

    ext_h = tile_h + 2 * HALO
    pitch = tile_w + 2 * HALO
    ext_rows = r * tile_h - HALO + jnp.arange(ext_h)
    ext_cols = c * tile_w - HALO + jnp.arange(pitch)
    row_ok = (ext_rows >= 0) & (ext_rows < n_row * tile_h)
    col_ok = (ext_cols >= 0) & (ext_cols < n_col * tile_w)
    valid = (row_ok[:, None] & col_ok[None, :]).reshape(-1)

    state = features
    for step in range(STEPS):
        page_rows = pages[step].T
        texture = page_rows.at[patch_index.reshape(-1)].get(mode="promise_in_bounds").T
        state = (
            state.reshape(chans, -1).astype(jnp.float32)
            + confidence.reshape(1, -1) * texture.astype(jnp.float32)
        ).astype(jnp.bfloat16).reshape(chans, tile_h, tile_w)
        x = exchange(state, HALO).reshape(chans, -1)
        lo = 0
        for block in range(LAYERS // 2):
            inner = jnp.maximum(conv_flat(x, conv_weight[2 * block], pitch), 0.0)
            lo += 1
            keep = valid[lo * pitch : (ext_h - lo) * pitch]
            inner = jnp.where(keep[None], inner, 0.0).astype(jnp.bfloat16)
            res = x[:, 2 * pitch : -2 * pitch].astype(jnp.float32) + conv_flat(inner, conv_weight[2 * block + 1], pitch)
            lo += 1
            keep = valid[lo * pitch : (ext_h - lo) * pitch]
            x = jnp.where(keep[None], res, 0.0).astype(jnp.bfloat16)
        state = x.reshape(chans, tile_h, pitch)[:, :, HALO : HALO + tile_w]
    return state


def solution(mesh):
    return jax.shard_map(
        body,
        mesh=mesh,
        in_specs=(
            P(None, "row", "col"),
            P("row", "col"),
            P("row", "col"),
            P(("row", "col"), None, None),
            P(),
            P(),
            P(),
        ),
        out_specs=P(None, "row", "col"),
        check_vma=False,
    )
```

```python
import jax
import jax.numpy as jnp
from jax import lax
from jax.sharding import PartitionSpec as P

LAYERS = 8
STEPS = 2
HALO = LAYERS


def shift_pairs(n_row, n_col, dr, dc):
    pairs = []
    for r in range(n_row):
        for c in range(n_col):
            tr, tc = r + dr, c + dc
            if 0 <= tr < n_row and 0 <= tc < n_col:
                pairs.append((r * n_col + c, tr * n_col + tc))
    return pairs


def exchange(block, width):
    n_row = lax.axis_size("row")
    n_col = lax.axis_size("col")
    axes = ("row", "col")
    rows = {-1: slice(block.shape[1] - width, None), 0: slice(None), 1: slice(0, width)}
    cols = {-1: slice(block.shape[2] - width, None), 0: slice(None), 1: slice(0, width)}
    got = {}
    for dr in (-1, 0, 1):
        for dc in (-1, 0, 1):
            if dr == 0 and dc == 0:
                continue
            piece = block[:, rows[dr], cols[dc]]
            moved = lax.ppermute(piece.reshape(piece.shape[0], -1), axes, shift_pairs(n_row, n_col, -dr, -dc))
            got[(dr, dc)] = moved.reshape(piece.shape)
    top = jnp.concatenate([got[(-1, -1)], got[(-1, 0)], got[(-1, 1)]], axis=2)
    mid = jnp.concatenate([got[(0, -1)], block, got[(0, 1)]], axis=2)
    bot = jnp.concatenate([got[(1, -1)], got[(1, 0)], got[(1, 1)]], axis=2)
    return jnp.concatenate([top, mid, bot], axis=1)


def broadcast_pages(masked):
    axes = ("row", "col")
    n = lax.axis_size("row") * lax.axis_size("col")
    steps, chans, width = masked.shape
    chunks = masked.reshape(steps, chans, n, width // n).transpose(2, 0, 1, 3)
    mine = lax.all_to_all(chunks, axes, 0, 0, tiled=True)
    total = jnp.sum(mine.astype(jnp.float32), axis=0).astype(masked.dtype)
    spread = jnp.broadcast_to(total[None], (n,) + total.shape)
    back = lax.all_to_all(spread, axes, 0, 0, tiled=True)
    return back.transpose(1, 2, 0, 3).reshape(steps, chans, width)


def conv_flat(flat, kernel, pitch):
    chans = flat.shape[0]
    rows = flat.shape[1] // pitch
    n_out = (rows - 2) * pitch
    padded = jnp.pad(flat, ((0, 0), (1, 1)))
    windows = [padded[:, dy * pitch + dx : dy * pitch + dx + n_out] for dy in range(3) for dx in range(3)]
    stacked = jnp.concatenate(windows, axis=0)
    flat_kernel = kernel.transpose(1, 0, 2).reshape(kernel.shape[1], 9 * chans)
    return jnp.dot(flat_kernel, stacked, preferred_element_type=jnp.float32)


def body(features, patch_index, confidence, bank, page_owner, texture_weight, conv_weight):
    chans, tile_h, tile_w = features.shape
    n_row = lax.axis_size("row")
    n_col = lax.axis_size("col")
    r = lax.axis_index("row")
    c = lax.axis_index("col")
    me = r * n_col + c

    local_proj = jnp.dot(texture_weight, bank[0], preferred_element_type=jnp.float32).astype(jnp.bfloat16)
    masked = jnp.stack(
        [jnp.where(me == page_owner[s], local_proj, jnp.zeros_like(local_proj)) for s in range(STEPS)]
    )
    pages = broadcast_pages(masked)

    ext_h = tile_h + 2 * HALO
    pitch = tile_w + 2 * HALO
    ext_rows = r * tile_h - HALO + jnp.arange(ext_h)
    ext_cols = c * tile_w - HALO + jnp.arange(pitch)
    row_ok = (ext_rows >= 0) & (ext_rows < n_row * tile_h)
    col_ok = (ext_cols >= 0) & (ext_cols < n_col * tile_w)
    valid = (row_ok[:, None] & col_ok[None, :]).reshape(-1)

    state = features
    for step in range(STEPS):
        one_hot = (patch_index.reshape(1, -1) == lax.broadcasted_iota(jnp.int32, (pages.shape[2], 1), 0)).astype(
            jnp.bfloat16
        )
        texture = jnp.dot(pages[step], one_hot, preferred_element_type=jnp.float32)
        state = (
            state.reshape(chans, -1).astype(jnp.float32)
            + confidence.reshape(1, -1) * texture.astype(jnp.float32)
        ).astype(jnp.bfloat16).reshape(chans, tile_h, tile_w)
        x = exchange(state, HALO).reshape(chans, -1)
        lo = 0
        for block in range(LAYERS // 2):
            inner = jnp.maximum(conv_flat(x, conv_weight[2 * block], pitch), 0.0)
            lo += 1
            keep = valid[lo * pitch : (ext_h - lo) * pitch]
            inner = jnp.where(keep[None], inner, 0.0).astype(jnp.bfloat16)
            res = x[:, 2 * pitch : -2 * pitch].astype(jnp.float32) + conv_flat(inner, conv_weight[2 * block + 1], pitch)
            lo += 1
            keep = valid[lo * pitch : (ext_h - lo) * pitch]
            x = jnp.where(keep[None], res, 0.0).astype(jnp.bfloat16)
        state = x.reshape(chans, tile_h, pitch)[:, :, HALO : HALO + tile_w]
    return state


def solution(mesh):
    return jax.shard_map(
        body,
        mesh=mesh,
        in_specs=(
            P(None, "row", "col"),
            P("row", "col"),
            P("row", "col"),
            P(("row", "col"), None, None),
            P(),
            P(),
            P(),
        ),
        out_specs=P(None, "row", "col"),
        check_vma=False,
    )
```

```python
import jax
import jax.numpy as jnp
from jax import lax
from jax.sharding import PartitionSpec as P

LAYERS = 8
STEPS = 2
HALO = LAYERS


def shift_pairs(n_row, n_col, dr, dc):
    pairs = []
    for r in range(n_row):
        for c in range(n_col):
            tr, tc = r + dr, c + dc
            if 0 <= tr < n_row and 0 <= tc < n_col:
                pairs.append((r * n_col + c, tr * n_col + tc))
    return pairs


def exchange(block, width):
    n_row = lax.axis_size("row")
    n_col = lax.axis_size("col")
    axes = ("row", "col")
    rows = {-1: slice(block.shape[1] - width, None), 0: slice(None), 1: slice(0, width)}
    cols = {-1: slice(block.shape[2] - width, None), 0: slice(None), 1: slice(0, width)}
    got = {}
    for dr in (-1, 0, 1):
        for dc in (-1, 0, 1):
            if dr == 0 and dc == 0:
                continue
            piece = block[:, rows[dr], cols[dc]]
            moved = lax.ppermute(piece.reshape(piece.shape[0], -1), axes, shift_pairs(n_row, n_col, -dr, -dc))
            got[(dr, dc)] = moved.reshape(piece.shape)
    top = jnp.concatenate([got[(-1, -1)], got[(-1, 0)], got[(-1, 1)]], axis=2)
    mid = jnp.concatenate([got[(0, -1)], block, got[(0, 1)]], axis=2)
    bot = jnp.concatenate([got[(1, -1)], got[(1, 0)], got[(1, 1)]], axis=2)
    return jnp.concatenate([top, mid, bot], axis=1)


def broadcast_pages(masked):
    axes = ("row", "col")
    n = lax.axis_size("row") * lax.axis_size("col")
    steps, chans, width = masked.shape
    chunks = masked.reshape(steps, chans, n, width // n).transpose(2, 0, 1, 3)
    mine = lax.all_to_all(chunks, axes, 0, 0, tiled=True)
    total = jnp.sum(mine.astype(jnp.float32), axis=0).astype(masked.dtype)
    spread = jnp.broadcast_to(total[None], (n,) + total.shape)
    back = lax.all_to_all(spread, axes, 0, 0, tiled=True)
    return back.transpose(1, 2, 0, 3).reshape(steps, chans, width)


def conv_flat(flat, kernel, pitch):
    chans = flat.shape[0]
    rows = flat.shape[1] // pitch
    n_out = (rows - 2) * pitch
    padded = jnp.pad(flat, ((0, 0), (1, 1)))
    windows = [padded[:, dy * pitch + dx : dy * pitch + dx + n_out] for dy in range(3) for dx in range(3)]
    stacked = jnp.concatenate(windows, axis=0)
    flat_kernel = kernel.transpose(1, 0, 2).reshape(kernel.shape[1], 9 * chans)
    return jnp.dot(flat_kernel, stacked, preferred_element_type=jnp.float32)


def body(features, patch_index, confidence, bank, page_owner, texture_weight, conv_weight):
    chans, tile_h, tile_w = features.shape
    n_row = lax.axis_size("row")
    n_col = lax.axis_size("col")
    r = lax.axis_index("row")
    c = lax.axis_index("col")
    me = r * n_col + c

    local_proj = jnp.dot(texture_weight, bank[0], preferred_element_type=jnp.float32).astype(jnp.bfloat16)
    masked = jnp.stack(
        [jnp.where(me == page_owner[s], local_proj, jnp.zeros_like(local_proj)) for s in range(STEPS)]
    )
    pages = broadcast_pages(masked)

    ext_h = tile_h + 2 * HALO
    pitch = tile_w + 2 * HALO
    ext_rows = r * tile_h - HALO + jnp.arange(ext_h)
    ext_cols = c * tile_w - HALO + jnp.arange(pitch)
    row_ok = (ext_rows >= 0) & (ext_rows < n_row * tile_h)
    col_ok = (ext_cols >= 0) & (ext_cols < n_col * tile_w)
    valid = (row_ok[:, None] & col_ok[None, :]).reshape(-1)

    feat_ext = exchange(features, HALO).reshape(chans, -1)
    aux = jnp.stack([confidence, patch_index.astype(jnp.float32)])
    aux_ext = exchange(aux, HALO).reshape(2, -1)

    def textured(base, conf, index, page):
        one_hot = (index.reshape(1, -1) == lax.broadcasted_iota(jnp.int32, (page.shape[1], 1), 0)).astype(
            jnp.bfloat16
        )
        texture = jnp.dot(page, one_hot, preferred_element_type=jnp.float32)
        return (base.astype(jnp.float32) + conf.reshape(1, -1) * texture).astype(jnp.bfloat16)

    state = None
    for step in range(STEPS):
        if step == 0:
            x = textured(feat_ext, aux_ext[0], aux_ext[1].astype(jnp.int32), pages[step])
        else:
            state = textured(state.reshape(chans, -1), confidence, patch_index, pages[step])
            x = exchange(state.reshape(chans, tile_h, tile_w), HALO).reshape(chans, -1)
        lo = 0
        for block in range(LAYERS // 2):
            inner = jnp.maximum(conv_flat(x, conv_weight[2 * block], pitch), 0.0)
            lo += 1
            keep = valid[lo * pitch : (ext_h - lo) * pitch]
            inner = jnp.where(keep[None], inner, 0.0).astype(jnp.bfloat16)
            res = x[:, 2 * pitch : -2 * pitch].astype(jnp.float32) + conv_flat(inner, conv_weight[2 * block + 1], pitch)
            lo += 1
            keep = valid[lo * pitch : (ext_h - lo) * pitch]
            x = jnp.where(keep[None], res, 0.0).astype(jnp.bfloat16)
        state = x.reshape(chans, tile_h, pitch)[:, :, HALO : HALO + tile_w]
    return state


def solution(mesh):
    return jax.shard_map(
        body,
        mesh=mesh,
        in_specs=(
            P(None, "row", "col"),
            P("row", "col"),
            P("row", "col"),
            P(("row", "col"), None, None),
            P(),
            P(),
            P(),
        ),
        out_specs=P(None, "row", "col"),
        check_vma=False,
    )
```

```python
import jax
import jax.numpy as jnp
from jax import lax
from jax.sharding import PartitionSpec as P

LAYERS = 8
STEPS = 2
HALO = LAYERS


def shift_pairs(n_row, n_col, dr, dc):
    pairs = []
    for r in range(n_row):
        for c in range(n_col):
            tr, tc = r + dr, c + dc
            if 0 <= tr < n_row and 0 <= tc < n_col:
                pairs.append((r * n_col + c, tr * n_col + tc))
    return pairs


def exchange(block, width):
    n_row = lax.axis_size("row")
    n_col = lax.axis_size("col")
    axes = ("row", "col")
    rows = {-1: slice(block.shape[1] - width, None), 0: slice(None), 1: slice(0, width)}
    cols = {-1: slice(block.shape[2] - width, None), 0: slice(None), 1: slice(0, width)}
    got = {}
    for dr in (-1, 0, 1):
        for dc in (-1, 0, 1):
            if dr == 0 and dc == 0:
                continue
            piece = block[:, rows[dr], cols[dc]]
            moved = lax.ppermute(piece.reshape(piece.shape[0], -1), axes, shift_pairs(n_row, n_col, -dr, -dc))
            got[(dr, dc)] = moved.reshape(piece.shape)
    top = jnp.concatenate([got[(-1, -1)], got[(-1, 0)], got[(-1, 1)]], axis=2)
    mid = jnp.concatenate([got[(0, -1)], block, got[(0, 1)]], axis=2)
    bot = jnp.concatenate([got[(1, -1)], got[(1, 0)], got[(1, 1)]], axis=2)
    return jnp.concatenate([top, mid, bot], axis=1)


def broadcast_pages(masked):
    axes = ("row", "col")
    n = lax.axis_size("row") * lax.axis_size("col")
    steps, chans, width = masked.shape
    chunks = masked.reshape(steps, chans, n, width // n).transpose(2, 0, 1, 3)
    mine = lax.all_to_all(chunks, axes, 0, 0, tiled=True)
    total = jnp.sum(mine.astype(jnp.float32), axis=0).astype(masked.dtype)
    spread = jnp.broadcast_to(total[None], (n,) + total.shape)
    back = lax.all_to_all(spread, axes, 0, 0, tiled=True)
    return back.transpose(1, 2, 0, 3).reshape(steps, chans, width)


def conv_flat(flat, kernel, pitch):
    chans = flat.shape[0]
    rows = flat.shape[1] // pitch
    n_out = (rows - 2) * pitch
    span = rows * pitch
    padded = jnp.pad(flat, ((0, 0), (1, 1)))
    shifted = jnp.concatenate([padded[:, dx : dx + span] for dx in range(3)], axis=0)
    total = None
    for dy in range(3):
        taps = kernel[3 * dy : 3 * dy + 3].transpose(1, 0, 2).reshape(kernel.shape[1], 3 * chans)
        part = jnp.dot(taps, shifted[:, dy * pitch : dy * pitch + n_out], preferred_element_type=jnp.float32)
        total = part if total is None else total + part
    return total


def body(features, patch_index, confidence, bank, page_owner, texture_weight, conv_weight):
    chans, tile_h, tile_w = features.shape
    n_row = lax.axis_size("row")
    n_col = lax.axis_size("col")
    r = lax.axis_index("row")
    c = lax.axis_index("col")
    me = r * n_col + c

    local_proj = jnp.dot(texture_weight, bank[0], preferred_element_type=jnp.float32).astype(jnp.bfloat16)
    masked = jnp.stack(
        [jnp.where(me == page_owner[s], local_proj, jnp.zeros_like(local_proj)) for s in range(STEPS)]
    )
    pages = broadcast_pages(masked)

    ext_h = tile_h + 2 * HALO
    pitch = tile_w + 2 * HALO
    ext_rows = r * tile_h - HALO + jnp.arange(ext_h)
    ext_cols = c * tile_w - HALO + jnp.arange(pitch)
    row_ok = (ext_rows >= 0) & (ext_rows < n_row * tile_h)
    col_ok = (ext_cols >= 0) & (ext_cols < n_col * tile_w)
    valid = (row_ok[:, None] & col_ok[None, :]).reshape(-1)

    state = features
    for step in range(STEPS):
        one_hot = (patch_index.reshape(1, -1) == lax.broadcasted_iota(jnp.int32, (pages.shape[2], 1), 0)).astype(
            jnp.bfloat16
        )
        texture = jnp.dot(pages[step], one_hot, preferred_element_type=jnp.float32)
        state = (
            state.reshape(chans, -1).astype(jnp.float32)
            + confidence.reshape(1, -1) * texture.astype(jnp.float32)
        ).astype(jnp.bfloat16).reshape(chans, tile_h, tile_w)
        x = exchange(state, HALO).reshape(chans, -1)
        lo = 0
        for block in range(LAYERS // 2):
            inner = jnp.maximum(conv_flat(x, conv_weight[2 * block], pitch), 0.0)
            lo += 1
            keep = valid[lo * pitch : (ext_h - lo) * pitch]
            inner = jnp.where(keep[None], inner, 0.0).astype(jnp.bfloat16)
            res = x[:, 2 * pitch : -2 * pitch].astype(jnp.float32) + conv_flat(inner, conv_weight[2 * block + 1], pitch)
            lo += 1
            keep = valid[lo * pitch : (ext_h - lo) * pitch]
            x = jnp.where(keep[None], res, 0.0).astype(jnp.bfloat16)
        state = x.reshape(chans, tile_h, pitch)[:, :, HALO : HALO + tile_w]
    return state


def solution(mesh):
    return jax.shard_map(
        body,
        mesh=mesh,
        in_specs=(
            P(None, "row", "col"),
            P("row", "col"),
            P("row", "col"),
            P(("row", "col"), None, None),
            P(),
            P(),
            P(),
        ),
        out_specs=P(None, "row", "col"),
        check_vma=False,
    )
```

```python
import jax
import jax.numpy as jnp
from jax import lax
from jax.sharding import PartitionSpec as P

LAYERS = 8
STEPS = 2
HALO = LAYERS


def shift_pairs(n_row, n_col, dr, dc):
    pairs = []
    for r in range(n_row):
        for c in range(n_col):
            tr, tc = r + dr, c + dc
            if 0 <= tr < n_row and 0 <= tc < n_col:
                pairs.append((r * n_col + c, tr * n_col + tc))
    return pairs


def exchange(block, width):
    n_row = lax.axis_size("row")
    n_col = lax.axis_size("col")
    axes = ("row", "col")
    rows = {-1: slice(block.shape[1] - width, None), 0: slice(None), 1: slice(0, width)}
    cols = {-1: slice(block.shape[2] - width, None), 0: slice(None), 1: slice(0, width)}
    got = {}
    for dr in (-1, 0, 1):
        for dc in (-1, 0, 1):
            if dr == 0 and dc == 0:
                continue
            piece = block[:, rows[dr], cols[dc]]
            moved = lax.ppermute(piece.reshape(piece.shape[0], -1), axes, shift_pairs(n_row, n_col, -dr, -dc))
            got[(dr, dc)] = moved.reshape(piece.shape)
    top = jnp.concatenate([got[(-1, -1)], got[(-1, 0)], got[(-1, 1)]], axis=2)
    mid = jnp.concatenate([got[(0, -1)], block, got[(0, 1)]], axis=2)
    bot = jnp.concatenate([got[(1, -1)], got[(1, 0)], got[(1, 1)]], axis=2)
    return jnp.concatenate([top, mid, bot], axis=1)


def broadcast_pages(masked):
    axes = ("row", "col")
    n = lax.axis_size("row") * lax.axis_size("col")
    steps, chans, width = masked.shape
    chunks = masked.reshape(steps, chans, n, width // n).transpose(2, 0, 1, 3)
    mine = lax.all_to_all(chunks, axes, 0, 0, tiled=True)
    total = jnp.sum(mine.astype(jnp.float32), axis=0).astype(masked.dtype)
    spread = jnp.broadcast_to(total[None], (n,) + total.shape)
    back = lax.all_to_all(spread, axes, 0, 0, tiled=True)
    return back.transpose(1, 2, 0, 3).reshape(steps, chans, width)


def conv_flat(flat, taps_by_row, pitch):
    chans = flat.shape[0]
    rows = flat.shape[1] // pitch
    n_out = (rows - 2) * pitch
    span = rows * pitch
    padded = jnp.pad(flat, ((0, 0), (1, 1)))
    shifted = jnp.concatenate([padded[:, dx : dx + span] for dx in range(3)], axis=0)
    total = None
    for dy in range(3):
        part = jnp.dot(taps_by_row[dy], shifted[:, dy * pitch : dy * pitch + n_out], preferred_element_type=jnp.float32)
        total = part if total is None else total + part
    return total


def body(features, patch_index, confidence, bank, page_owner, texture_weight, conv_weight):
    chans, tile_h, tile_w = features.shape
    n_row = lax.axis_size("row")
    n_col = lax.axis_size("col")
    r = lax.axis_index("row")
    c = lax.axis_index("col")
    me = r * n_col + c

    local_proj = jnp.dot(texture_weight, bank[0], preferred_element_type=jnp.float32).astype(jnp.bfloat16)
    masked = jnp.stack(
        [jnp.where(me == page_owner[s], local_proj, jnp.zeros_like(local_proj)) for s in range(STEPS)]
    )
    pages = broadcast_pages(masked)

    ext_h = tile_h + 2 * HALO
    pitch = tile_w + 2 * HALO
    ext_rows = r * tile_h - HALO + jnp.arange(ext_h)
    ext_cols = c * tile_w - HALO + jnp.arange(pitch)
    row_ok = (ext_rows >= 0) & (ext_rows < n_row * tile_h)
    col_ok = (ext_cols >= 0) & (ext_cols < n_col * tile_w)
    valid = (row_ok[:, None] & col_ok[None, :]).reshape(-1)

    layers, _, c_out, c_in = conv_weight.shape
    weights = conv_weight.reshape(layers, 3, 3, c_out, c_in).transpose(0, 1, 3, 2, 4).reshape(layers, 3, c_out, 3 * c_in)

    state = features
    for step in range(STEPS):
        one_hot = (patch_index.reshape(1, -1) == lax.broadcasted_iota(jnp.int32, (pages.shape[2], 1), 0)).astype(
            jnp.bfloat16
        )
        texture = jnp.dot(pages[step], one_hot, preferred_element_type=jnp.float32)
        state = (
            state.reshape(chans, -1).astype(jnp.float32)
            + confidence.reshape(1, -1) * texture.astype(jnp.float32)
        ).astype(jnp.bfloat16).reshape(chans, tile_h, tile_w)
        x = exchange(state, HALO).reshape(chans, -1)
        lo = 0
        for block in range(LAYERS // 2):
            inner = jnp.maximum(conv_flat(x, weights[2 * block], pitch), 0.0)
            lo += 1
            keep = valid[lo * pitch : (ext_h - lo) * pitch]
            inner = jnp.where(keep[None], inner, 0.0).astype(jnp.bfloat16)
            res = x[:, 2 * pitch : -2 * pitch].astype(jnp.float32) + conv_flat(inner, weights[2 * block + 1], pitch)
            lo += 1
            keep = valid[lo * pitch : (ext_h - lo) * pitch]
            x = jnp.where(keep[None], res, 0.0).astype(jnp.bfloat16)
        state = x.reshape(chans, tile_h, pitch)[:, :, HALO : HALO + tile_w]
    return state


def solution(mesh):
    return jax.shard_map(
        body,
        mesh=mesh,
        in_specs=(
            P(None, "row", "col"),
            P("row", "col"),
            P("row", "col"),
            P(("row", "col"), None, None),
            P(),
            P(),
            P(),
        ),
        out_specs=P(None, "row", "col"),
        check_vma=False,
    )
```

```python
import jax
import jax.numpy as jnp
from jax import lax
from jax.sharding import PartitionSpec as P

LAYERS = 8
STEPS = 2
HALO = LAYERS


def shift_pairs(n_row, n_col, dr, dc):
    pairs = []
    for r in range(n_row):
        for c in range(n_col):
            tr, tc = r + dr, c + dc
            if 0 <= tr < n_row and 0 <= tc < n_col:
                pairs.append((r * n_col + c, tr * n_col + tc))
    return pairs


def exchange(block, width):
    def along(block, axis, dim):
        count = lax.axis_size(axis)
        size = block.shape[dim]
        forward = [(i, i + 1) for i in range(count - 1)]
        backward = [(i + 1, i) for i in range(count - 1)]
        low_edge = lax.slice_in_dim(block, size - width, size, axis=dim)
        high_edge = lax.slice_in_dim(block, 0, width, axis=dim)
        low = lax.ppermute(low_edge.reshape(block.shape[0], -1), axis, forward).reshape(low_edge.shape)
        high = lax.ppermute(high_edge.reshape(block.shape[0], -1), axis, backward).reshape(high_edge.shape)
        return jnp.concatenate([low, block, high], axis=dim)

    return along(along(block, "row", 1), "col", 2)


def broadcast_pages(masked):
    axes = ("row", "col")
    n = lax.axis_size("row") * lax.axis_size("col")
    steps, chans, width = masked.shape
    chunks = masked.reshape(steps, chans, n, width // n).transpose(2, 0, 1, 3)
    mine = lax.all_to_all(chunks, axes, 0, 0, tiled=True)
    total = jnp.sum(mine.astype(jnp.float32), axis=0).astype(masked.dtype)
    spread = jnp.broadcast_to(total[None], (n,) + total.shape)
    back = lax.all_to_all(spread, axes, 0, 0, tiled=True)
    return back.transpose(1, 2, 0, 3).reshape(steps, chans, width)


def conv_flat(flat, taps_by_row, pitch):
    chans = flat.shape[0]
    rows = flat.shape[1] // pitch
    n_out = (rows - 2) * pitch
    span = rows * pitch
    padded = jnp.pad(flat, ((0, 0), (1, 1)))
    shifted = jnp.concatenate([padded[:, dx : dx + span] for dx in range(3)], axis=0)
    total = None
    for dy in range(3):
        part = jnp.dot(taps_by_row[dy], shifted[:, dy * pitch : dy * pitch + n_out], preferred_element_type=jnp.float32)
        total = part if total is None else total + part
    return total


def body(features, patch_index, confidence, bank, page_owner, texture_weight, conv_weight):
    chans, tile_h, tile_w = features.shape
    n_row = lax.axis_size("row")
    n_col = lax.axis_size("col")
    r = lax.axis_index("row")
    c = lax.axis_index("col")
    me = r * n_col + c

    local_proj = jnp.dot(texture_weight, bank[0], preferred_element_type=jnp.float32).astype(jnp.bfloat16)
    masked = jnp.stack(
        [jnp.where(me == page_owner[s], local_proj, jnp.zeros_like(local_proj)) for s in range(STEPS)]
    )
    pages = broadcast_pages(masked)

    ext_h = tile_h + 2 * HALO
    pitch = tile_w + 2 * HALO
    ext_rows = r * tile_h - HALO + jnp.arange(ext_h)
    ext_cols = c * tile_w - HALO + jnp.arange(pitch)
    row_ok = (ext_rows >= 0) & (ext_rows < n_row * tile_h)
    col_ok = (ext_cols >= 0) & (ext_cols < n_col * tile_w)
    valid = (row_ok[:, None] & col_ok[None, :]).reshape(-1)

    layers, _, c_out, c_in = conv_weight.shape
    weights = conv_weight.reshape(layers, 3, 3, c_out, c_in).transpose(0, 1, 3, 2, 4).reshape(layers, 3, c_out, 3 * c_in)

    state = features
    for step in range(STEPS):
        one_hot = (patch_index.reshape(1, -1) == lax.broadcasted_iota(jnp.int32, (pages.shape[2], 1), 0)).astype(
            jnp.bfloat16
        )
        texture = jnp.dot(pages[step], one_hot, preferred_element_type=jnp.float32)
        state = (
            state.reshape(chans, -1).astype(jnp.float32)
            + confidence.reshape(1, -1) * texture.astype(jnp.float32)
        ).astype(jnp.bfloat16).reshape(chans, tile_h, tile_w)
        x = exchange(state, HALO).reshape(chans, -1)
        lo = 0
        for block in range(LAYERS // 2):
            inner = jnp.maximum(conv_flat(x, weights[2 * block], pitch), 0.0)
            lo += 1
            keep = valid[lo * pitch : (ext_h - lo) * pitch]
            inner = jnp.where(keep[None], inner, 0.0).astype(jnp.bfloat16)
            res = x[:, 2 * pitch : -2 * pitch].astype(jnp.float32) + conv_flat(inner, weights[2 * block + 1], pitch)
            lo += 1
            keep = valid[lo * pitch : (ext_h - lo) * pitch]
            x = jnp.where(keep[None], res, 0.0).astype(jnp.bfloat16)
        state = x.reshape(chans, tile_h, pitch)[:, :, HALO : HALO + tile_w]
    return state


def solution(mesh):
    return jax.shard_map(
        body,
        mesh=mesh,
        in_specs=(
            P(None, "row", "col"),
            P("row", "col"),
            P("row", "col"),
            P(("row", "col"), None, None),
            P(),
            P(),
            P(),
        ),
        out_specs=P(None, "row", "col"),
        check_vma=False,
    )
```

```python
import jax
import jax.numpy as jnp
from jax import lax
from jax.sharding import PartitionSpec as P

LAYERS = 8
STEPS = 2
HALO = LAYERS


def shift_pairs(n_row, n_col, dr, dc):
    pairs = []
    for r in range(n_row):
        for c in range(n_col):
            tr, tc = r + dr, c + dc
            if 0 <= tr < n_row and 0 <= tc < n_col:
                pairs.append((r * n_col + c, tr * n_col + tc))
    return pairs


def exchange(block, width):
    def along(block, axis, dim):
        count = lax.axis_size(axis)
        size = block.shape[dim]
        forward = [(i, i + 1) for i in range(count - 1)]
        backward = [(i + 1, i) for i in range(count - 1)]
        low_edge = lax.slice_in_dim(block, size - width, size, axis=dim)
        high_edge = lax.slice_in_dim(block, 0, width, axis=dim)
        low = lax.ppermute(low_edge.reshape(block.shape[0], -1), axis, forward).reshape(low_edge.shape)
        high = lax.ppermute(high_edge.reshape(block.shape[0], -1), axis, backward).reshape(high_edge.shape)
        return jnp.concatenate([low, block, high], axis=dim)

    return along(along(block, "row", 1), "col", 2)


def broadcast_pages(masked):
    axes = ("row", "col")
    n = lax.axis_size("row") * lax.axis_size("col")
    steps, chans, width = masked.shape
    chunks = masked.reshape(steps, chans, n, width // n).transpose(2, 0, 1, 3)
    mine = lax.all_to_all(chunks, axes, 0, 0, tiled=True)
    total = jnp.sum(mine.astype(jnp.float32), axis=0).astype(masked.dtype)
    spread = jnp.broadcast_to(total[None], (n,) + total.shape)
    back = lax.all_to_all(spread, axes, 0, 0, tiled=True)
    return back.transpose(1, 2, 0, 3).reshape(steps, chans, width)


def conv_flat(flat, taps_by_row, pitch):
    chans = flat.shape[0]
    rows = flat.shape[1] // pitch
    n_out = (rows - 2) * pitch
    span = rows * pitch
    padded = jnp.pad(flat, ((0, 0), (1, 1)))
    shifted = jnp.concatenate([padded[:, dx : dx + span] for dx in range(3)], axis=0)
    total = None
    for dy in range(3):
        part = jnp.dot(taps_by_row[dy], shifted[:, dy * pitch : dy * pitch + n_out], preferred_element_type=jnp.float32)
        total = part if total is None else total + part
    return total


def body(features, patch_index, confidence, bank, page_owner, texture_weight, conv_weight):
    chans, tile_h, tile_w = features.shape
    n_row = lax.axis_size("row")
    n_col = lax.axis_size("col")
    r = lax.axis_index("row")
    c = lax.axis_index("col")
    me = r * n_col + c

    local_proj = jnp.dot(texture_weight, bank[0], preferred_element_type=jnp.float32).astype(jnp.bfloat16)
    masked = jnp.stack(
        [jnp.where(me == page_owner[s], local_proj, jnp.zeros_like(local_proj)) for s in range(STEPS)]
    )
    pages = broadcast_pages(masked)

    ext_h = tile_h + 2 * HALO
    pitch = tile_w + 2 * HALO
    ext_rows = r * tile_h - HALO + jnp.arange(ext_h)
    ext_cols = c * tile_w - HALO + jnp.arange(pitch)
    row_ok = (ext_rows >= 0) & (ext_rows < n_row * tile_h)
    col_ok = (ext_cols >= 0) & (ext_cols < n_col * tile_w)
    valid = (row_ok[:, None] & col_ok[None, :]).reshape(-1)

    layers, _, c_out, c_in = conv_weight.shape
    weights = conv_weight.reshape(layers, 3, 3, c_out, c_in).transpose(0, 1, 3, 2, 4).reshape(layers, 3, c_out, 3 * c_in)

    one_hot = (patch_index.reshape(1, -1) == lax.broadcasted_iota(jnp.int32, (pages.shape[2], 1), 0)).astype(
        jnp.bfloat16
    )
    textures = jnp.dot(
        pages.reshape(STEPS * chans, -1), one_hot, preferred_element_type=jnp.float32
    ).astype(jnp.bfloat16).reshape(STEPS, chans, -1)

    state = features
    for step in range(STEPS):
        state = (
            state.reshape(chans, -1).astype(jnp.float32)
            + confidence.reshape(1, -1) * textures[step].astype(jnp.float32)
        ).astype(jnp.bfloat16).reshape(chans, tile_h, tile_w)
        x = exchange(state, HALO).reshape(chans, -1)
        lo = 0
        for block in range(LAYERS // 2):
            inner = jnp.maximum(conv_flat(x, weights[2 * block], pitch), 0.0)
            lo += 1
            keep = valid[lo * pitch : (ext_h - lo) * pitch]
            inner = jnp.where(keep[None], inner, 0.0).astype(jnp.bfloat16)
            res = x[:, 2 * pitch : -2 * pitch].astype(jnp.float32) + conv_flat(inner, weights[2 * block + 1], pitch)
            lo += 1
            keep = valid[lo * pitch : (ext_h - lo) * pitch]
            x = jnp.where(keep[None], res, 0.0).astype(jnp.bfloat16)
        state = x.reshape(chans, tile_h, pitch)[:, :, HALO : HALO + tile_w]
    return state


def solution(mesh):
    return jax.shard_map(
        body,
        mesh=mesh,
        in_specs=(
            P(None, "row", "col"),
            P("row", "col"),
            P("row", "col"),
            P(("row", "col"), None, None),
            P(),
            P(),
            P(),
        ),
        out_specs=P(None, "row", "col"),
        check_vma=False,
    )
```

```python
import jax
import jax.numpy as jnp
from jax import lax
from jax.sharding import PartitionSpec as P


LAYERS = 8
STEPS = 2
HALO = LAYERS


def exchange(block, width):
    def along(block, axis, dim):
        count = lax.axis_size(axis)
        size = block.shape[dim]
        forward = [(i, i + 1) for i in range(count - 1)]
        backward = [(i + 1, i) for i in range(count - 1)]
        low_edge = lax.slice_in_dim(block, size - width, size, axis=dim)
        high_edge = lax.slice_in_dim(block, 0, width, axis=dim)
        low = lax.ppermute(low_edge.reshape(block.shape[0], -1), axis, forward).reshape(low_edge.shape)
        high = lax.ppermute(high_edge.reshape(block.shape[0], -1), axis, backward).reshape(high_edge.shape)
        return jnp.concatenate([low, block, high], axis=dim)

    block = along(block, "row", 1)
    return along(block, "col", 2)


def broadcast_pages(masked):
    axes = ("row", "col")
    n = lax.axis_size("row") * lax.axis_size("col")
    steps, chans, width = masked.shape
    chunks = masked.reshape(steps, chans, n, width // n).transpose(2, 0, 1, 3)
    mine = lax.all_to_all(chunks, axes, 0, 0, tiled=True)
    total = jnp.sum(mine.astype(jnp.float32), axis=0).astype(masked.dtype)
    spread = jnp.broadcast_to(total[None], (n,) + total.shape)
    back = lax.all_to_all(spread, axes, 0, 0, tiled=True)
    return back.transpose(1, 2, 0, 3).reshape(steps, chans, width)


def conv_flat(flat, taps_by_row, pitch):
    rows = flat.shape[1] // pitch
    n_out = (rows - 2) * pitch
    span = rows * pitch
    padded = jnp.pad(flat, ((0, 0), (1, 1)))
    shifted = jnp.concatenate([padded[:, dx : dx + span] for dx in range(3)], axis=0)
    total = None
    for dy in range(3):
        part = jnp.dot(taps_by_row[dy], shifted[:, dy * pitch : dy * pitch + n_out], preferred_element_type=jnp.float32)
        total = part if total is None else total + part
    return total


def body(features, patch_index, confidence, bank, page_owner, texture_weight, conv_weight):
    chans, tile_h, tile_w = features.shape
    n_row = lax.axis_size("row")
    n_col = lax.axis_size("col")
    r = lax.axis_index("row")
    c = lax.axis_index("col")
    me = r * n_col + c

    local_proj = jnp.dot(texture_weight, bank[0], preferred_element_type=jnp.float32).astype(jnp.bfloat16)
    masked = jnp.stack(
        [jnp.where(me == page_owner[s], local_proj, jnp.zeros_like(local_proj)) for s in range(STEPS)]
    )
    pages = broadcast_pages(masked)

    ext_h = tile_h + 2 * HALO
    pitch = tile_w + 2 * HALO
    ext_rows = r * tile_h - HALO + jnp.arange(ext_h)
    ext_cols = c * tile_w - HALO + jnp.arange(pitch)
    row_ok = (ext_rows >= 0) & (ext_rows < n_row * tile_h)
    col_ok = (ext_cols >= 0) & (ext_cols < n_col * tile_w)
    valid = (row_ok[:, None] & col_ok[None, :]).reshape(-1)

    layers, _, c_out, c_in = conv_weight.shape
    weights = conv_weight.reshape(layers, 3, 3, c_out, c_in).transpose(0, 1, 3, 2, 4).reshape(layers, 3, c_out, 3 * c_in)

    def texture_of(step):
        one_hot = (patch_index.reshape(1, -1) == lax.broadcasted_iota(jnp.int32, (pages.shape[2], 1), 0)).astype(
            jnp.bfloat16
        )
        texture = jnp.dot(pages[step], one_hot, preferred_element_type=jnp.float32).astype(jnp.bfloat16)
        return lax.optimization_barrier(texture)

    textures = [texture_of(step) for step in range(STEPS)]
    state = features
    for step in range(STEPS):
        state = (
            state.reshape(chans, -1).astype(jnp.float32)
            + confidence.reshape(1, -1) * textures[step].astype(jnp.float32)
        ).astype(jnp.bfloat16).reshape(chans, tile_h, tile_w)
        x = exchange(state, HALO).reshape(chans, -1)
        lo = 0
        for block in range(LAYERS // 2):
            inner = jnp.maximum(conv_flat(x, weights[2 * block], pitch), 0.0)
            lo += 1
            keep = valid[lo * pitch : (ext_h - lo) * pitch]
            inner = jnp.where(keep[None], inner, 0.0).astype(jnp.bfloat16)
            res = x[:, 2 * pitch : -2 * pitch].astype(jnp.float32) + conv_flat(inner, weights[2 * block + 1], pitch)
            lo += 1
            keep = valid[lo * pitch : (ext_h - lo) * pitch]
            x = jnp.where(keep[None], res, 0.0).astype(jnp.bfloat16)
        state = x.reshape(chans, tile_h, pitch)[:, :, HALO : HALO + tile_w]
    return state


def solution(mesh):
    return jax.shard_map(
        body,
        mesh=mesh,
        in_specs=(
            P(None, "row", "col"),
            P("row", "col"),
            P("row", "col"),
            P(("row", "col"), None, None),
            P(),
            P(),
            P(),
        ),
        out_specs=P(None, "row", "col"),
        check_vma=False,
    )
```

```python
import jax
import jax.numpy as jnp
from jax import lax
from jax.sharding import PartitionSpec as P

LAYERS = 8
STEPS = 2
HALO = LAYERS


def shift_pairs(n_row, n_col, dr, dc):
    pairs = []
    for r in range(n_row):
        for c in range(n_col):
            tr, tc = r + dr, c + dc
            if 0 <= tr < n_row and 0 <= tc < n_col:
                pairs.append((r * n_col + c, tr * n_col + tc))
    return pairs


def exchange(block, width):
    def along(block, axis, dim):
        count = lax.axis_size(axis)
        size = block.shape[dim]
        forward = [(i, i + 1) for i in range(count - 1)]
        backward = [(i + 1, i) for i in range(count - 1)]
        low_edge = lax.slice_in_dim(block, size - width, size, axis=dim)
        high_edge = lax.slice_in_dim(block, 0, width, axis=dim)
        low = lax.ppermute(low_edge.reshape(block.shape[0], -1), axis, forward).reshape(low_edge.shape)
        high = lax.ppermute(high_edge.reshape(block.shape[0], -1), axis, backward).reshape(high_edge.shape)
        return jnp.concatenate([low, block, high], axis=dim)

    return along(along(block, "row", 1), "col", 2)


def broadcast_pages(masked):
    axes = ("row", "col")
    n = lax.axis_size("row") * lax.axis_size("col")
    steps, chans, width = masked.shape
    chunks = masked.reshape(steps, chans, n, width // n).transpose(2, 0, 1, 3)
    mine = lax.all_to_all(chunks, axes, 0, 0, tiled=True)
    total = jnp.sum(mine.astype(jnp.float32), axis=0).astype(masked.dtype)
    spread = jnp.broadcast_to(total[None], (n,) + total.shape)
    back = lax.all_to_all(spread, axes, 0, 0, tiled=True)
    return back.transpose(1, 2, 0, 3).reshape(steps, chans, width)


def conv_flat(flat, taps_by_row, pitch):
    chans = flat.shape[0]
    rows = flat.shape[1] // pitch
    n_out = (rows - 2) * pitch
    span = rows * pitch
    padded = jnp.pad(flat, ((0, 0), (1, 1)))
    shifted = jnp.concatenate([padded[:, dx : dx + span] for dx in range(3)], axis=0)
    total = None
    for dy in range(3):
        part = jnp.dot(taps_by_row[dy], shifted[:, dy * pitch : dy * pitch + n_out], preferred_element_type=jnp.float32)
        total = part if total is None else total + part
    return total


def body(features, patch_index, confidence, bank, page_owner, texture_weight, conv_weight):
    chans, tile_h, tile_w = features.shape
    n_row = lax.axis_size("row")
    n_col = lax.axis_size("col")
    r = lax.axis_index("row")
    c = lax.axis_index("col")
    me = r * n_col + c

    local_proj = jnp.dot(texture_weight, bank[0], preferred_element_type=jnp.float32).astype(jnp.bfloat16)
    masked = jnp.stack(
        [jnp.where(me == page_owner[s], local_proj, jnp.zeros_like(local_proj)) for s in range(STEPS)]
    )
    pages = broadcast_pages(masked)

    ext_h = tile_h + 2 * HALO
    pitch = tile_w + 2 * HALO
    ext_rows = r * tile_h - HALO + jnp.arange(ext_h)
    ext_cols = c * tile_w - HALO + jnp.arange(pitch)
    row_ok = (ext_rows >= 0) & (ext_rows < n_row * tile_h)
    col_ok = (ext_cols >= 0) & (ext_cols < n_col * tile_w)
    valid = (row_ok[:, None] & col_ok[None, :]).reshape(-1)

    layers, _, c_out, c_in = conv_weight.shape
    weights = conv_weight.reshape(layers, 3, 3, c_out, c_in).transpose(0, 1, 3, 2, 4).reshape(layers, 3, c_out, 3 * c_in)

    def one_step(step, state):
        one_hot = (patch_index.reshape(1, -1) == lax.broadcasted_iota(jnp.int32, (pages.shape[2], 1), 0)).astype(
            jnp.bfloat16
        )
        texture = jnp.dot(pages[step], one_hot, preferred_element_type=jnp.float32)
        state = (
            state.reshape(chans, -1).astype(jnp.float32)
            + confidence.reshape(1, -1) * texture.astype(jnp.float32)
        ).astype(jnp.bfloat16).reshape(chans, tile_h, tile_w)
        x = exchange(state, HALO).reshape(chans, -1)
        lo = 0
        for block in range(LAYERS // 2):
            inner = jnp.maximum(conv_flat(x, weights[2 * block], pitch), 0.0)
            lo += 1
            keep = valid[lo * pitch : (ext_h - lo) * pitch]
            inner = jnp.where(keep[None], inner, 0.0).astype(jnp.bfloat16)
            res = x[:, 2 * pitch : -2 * pitch].astype(jnp.float32) + conv_flat(inner, weights[2 * block + 1], pitch)
            lo += 1
            keep = valid[lo * pitch : (ext_h - lo) * pitch]
            x = jnp.where(keep[None], res, 0.0).astype(jnp.bfloat16)
        return x.reshape(chans, tile_h, pitch)[:, :, HALO : HALO + tile_w]

    state = lax.fori_loop(0, STEPS, one_step, features)
    return state


def solution(mesh):
    return jax.shard_map(
        body,
        mesh=mesh,
        in_specs=(
            P(None, "row", "col"),
            P("row", "col"),
            P("row", "col"),
            P(("row", "col"), None, None),
            P(),
            P(),
            P(),
        ),
        out_specs=P(None, "row", "col"),
        check_vma=False,
    )
```
